128 devices in a mesh: grp: 8 (over z_lo, x), blk: 16 (over z_hi, y, core).
Axes of the slice: x: 4, y: 4, z: 4 (z_hi: 2, z_lo: 2; z = z_hi * 2 + z_lo), core: 2. Of those that a mesh axis runs over, the one named last changes fastest.
Arguments:
- matrix: bfloat16 [16384, 16384], P('blk', 'grp')
- panels: bfloat16 [16384, 4096], P('grp', 'blk')
- pattern: int32 [128, 128], replicated, may hold values from 0 to 1, as said below
- pruned: int32 [128, 32], replicated, may hold values from 0 to 1, as said below
- owners: int32 [32], replicated, may hold values from 0 to 31, each once
Outputs:
- owned: float32 [16, 8, 128, 4096], P(None, 'grp', None, 'blk')
The draws below stay inside these ranges and needn't reach their ends.
Inputs may be any that keep to these rules, and one draw needn't show every extreme that they name: `pattern`: 0 or 1; every diagonal block is 1. `pruned`: 0 or 1; block (c, c) is 1 for every window column block c; every block row holds exactly 16 ones. `owners`: each slot once.
All inputs are finite; a program needn't handle non-finite values.
Results may differ from the reference program's by a relative error of at most 0.0003.
Values may be sent and summed in bfloat16 or wider, within the bound.
No kernel may reach another device: no remote copies, remote signals or barrier semaphores. Data moves between devices by JAX's collectives and lax.ppermute only.
A program may use at most 128 MiB of HBM per device.

```python
import math
import jax
import jax.numpy as jnp

BS = 128
N = 16384
NB = 128
W = 4096
WB = 32
SUB = 128
N_GRP = 8
N_BLK = 16


def rough_values(key, rows, cols):
    values = jnp.exp(jax.random.uniform(key, (rows, cols), jnp.float32, math.log(0.1), math.log(10.0)))
    scale = 1.0 + 2.0 * jnp.arange(rows, dtype=jnp.float32) / (rows - 1)
    return values * scale[:, None]


def draw_matrix(key, part):
    return rough_values(jax.random.fold_in(key, 11), N, N).astype(jnp.bfloat16)


def draw_panels(key, part):
    return rough_values(jax.random.fold_in(key, 23), N, W).astype(jnp.bfloat16)


def draw_pattern(key, part):
    level_key, entry_key = jax.random.split(jax.random.fold_in(key, 37))
    levels = jax.random.randint(level_key, (1, NB), 15, 66)
    entries = jax.random.randint(entry_key, (NB, NB), 0, 100)
    stored = (entries < levels).astype(jnp.int32)
    diagonal = (jnp.arange(NB)[:, None] == jnp.arange(NB)[None, :]).astype(jnp.int32)
    return jnp.maximum(stored, diagonal)


def draw_pruned(key, part):
    raw = jax.random.randint(jax.random.fold_in(key, 41), (NB, WB), 0, 1048576)
    columns = jnp.arange(WB, dtype=jnp.int32)
    diagonal = (jnp.arange(NB, dtype=jnp.int32)[:, None] == columns[None, :]).astype(jnp.int32)
    scores = raw * WB + columns[None, :] + diagonal * (1048576 * WB)
    order = jnp.argsort(-scores, axis=1)
    ranks = jnp.argsort(order, axis=1)
    return (ranks < WB // 2).astype(jnp.int32)


def setup_inputs(seed: int = 0) -> dict:
    key_of = jax.random.split(jax.random.key(seed), 6)
    return {
        "matrix": draw_matrix(jax.random.fold_in(key_of[5], 71), 0),
        "panels": draw_panels(jax.random.fold_in(key_of[5], 71), 0),
        "pattern": draw_pattern(jax.random.fold_in(key_of[5], 71), 0),
        "pruned": draw_pruned(jax.random.fold_in(key_of[5], 71), 0),
        "owners": jax.random.permutation(key_of[4], WB).astype(jnp.int32),
    }


def reference(matrix, panels, pattern, pruned, owners):
    block_rows = N // BS
    window_blocks = W // BS
    left = (matrix.reshape(block_rows, BS, block_rows, BS) * pattern.astype(matrix.dtype)[:, None, :, None]).reshape(N, N)
    right_mask = pattern[:, :window_blocks].astype(panels.dtype)
    right = (panels.reshape(block_rows, BS, window_blocks, BS) * right_mask[:, None, :, None]).reshape(N, W)
    expanded = jnp.dot(left, right, preferred_element_type=jnp.float32)
    inflated = expanded * expanded
    kept = (inflated.reshape(block_rows, BS, window_blocks, BS) * pruned.astype(inflated.dtype)[:, None, :, None]).reshape(N, W)
    totals = jnp.sum(kept, axis=0)
    normalized = N * kept / totals
    inverse = jnp.zeros((window_blocks,), jnp.int32).at[owners].set(jnp.arange(window_blocks, dtype=jnp.int32))
    arranged = normalized.reshape(N_BLK, N_GRP, SUB, window_blocks, BS)[:, :, :, inverse, :]
    return arranged.reshape(N_BLK, N_GRP, SUB, W)
```

```python
import jax
import jax.numpy as jnp
from jax import lax
from jax.sharding import Mesh
from jax.sharding import PartitionSpec as P

BS = 128
BLK = ("blk_0", "blk_1", "blk_2")
GRP = ("grp_0", "grp_1")
GRP_BLK = ("grp_0", "grp_1", "blk_0", "blk_1", "blk_2")
REMOTE = ("blk_0", "blk_1")
CORE = "blk_2"


def shards(matrix, panels, pattern, pruned, owners):
    blk_count = lax.axis_size(BLK)
    blk_id = lax.axis_index(BLK)
    grp_id = lax.axis_index(GRP)
    core_count = lax.axis_size(CORE)
    remote_count = lax.axis_size(REMOTE)
    row_count, inner = matrix.shape
    panel_width = panels.shape[1]
    row_blocks = row_count // BS
    inner_blocks = inner // BS
    panel_blocks = panel_width // BS
    width_total = panel_width * blk_count
    window_blocks = width_total // BS
    half_blocks = window_blocks // 2
    tile_left = lax.dynamic_slice(
        pattern, (blk_id * row_blocks, grp_id * inner_blocks), (row_blocks, inner_blocks)
    ).astype(jnp.bfloat16)
    left = (matrix.reshape(row_blocks, BS, inner_blocks, BS) * tile_left[:, None, :, None]).reshape(
        row_count, inner
    )
    tile_right = lax.dynamic_slice(
        pattern, (grp_id * inner_blocks, blk_id * panel_blocks), (inner_blocks, panel_blocks)
    ).astype(jnp.bfloat16)
    right = (
        panels.reshape(inner_blocks, BS, panel_blocks, BS) * tile_right[:, None, :, None]
    ).reshape(inner, panel_width)
    gathered = lax.all_gather(right, REMOTE, axis=1, tiled=True)
    gathered = lax.all_gather(gathered, CORE, axis=1, tiled=True)
    column_ids = jnp.arange(window_blocks, dtype=jnp.int32)
    src_blk = column_ids // panel_blocks
    position = (
        (src_blk % core_count) * remote_count + src_blk // core_count
    ) * panel_blocks + column_ids % panel_blocks
    partial_value = jnp.dot(left, gathered, preferred_element_type=jnp.float32)
    local_pruned = lax.dynamic_slice_in_dim(pruned, blk_id * row_blocks, row_blocks, 0)
    listing = jnp.argsort((1 - local_pruned) * window_blocks + column_ids[None, :], axis=1)[
        :, :half_blocks
    ]
    blocked = partial_value.reshape(row_blocks, BS, window_blocks, BS)
    packed = jnp.take_along_axis(blocked, position[listing][:, None, :, None], axis=2).reshape(
        row_count, half_blocks * BS
    )
    summed_packed = lax.psum_scatter(packed, GRP, scatter_dimension=0, tiled=True)
    piece_rows = row_count // lax.axis_size(GRP)
    row_block = (blk_id * row_count + grp_id * piece_rows) // BS
    row_pruned = lax.dynamic_index_in_dim(pruned, row_block, 0, keepdims=False)
    slot_of = jnp.clip(jnp.cumsum(row_pruned) - 1, 0, half_blocks - 1)
    squared = summed_packed.reshape(piece_rows, half_blocks, BS)
    squared = squared * squared
    local_totals = jnp.sum(squared, axis=0)[slot_of] * row_pruned.astype(jnp.float32)[:, None]
    totals = lax.psum(local_totals, GRP_BLK)
    inverse = (
        jnp.zeros((window_blocks,), jnp.int32)
        .at[owners]
        .set(jnp.arange(window_blocks, dtype=jnp.int32))
    )
    picked = jnp.take(squared, slot_of[inverse], axis=1)
    kept = picked * row_pruned[inverse].astype(jnp.float32)[None, :, None]
    normalized = (row_count * blk_count) * kept / totals[inverse][None, :, :]
    arranged = normalized.reshape(1, piece_rows, width_total)
    moved = lax.all_to_all(arranged, BLK, split_axis=2, concat_axis=0, tiled=True)
    return moved[:, None, :, :]


def solution(mesh):
    split = Mesh(mesh.devices.reshape(2, 4, 2, 4, 2), ("grp_0", "grp_1", "blk_0", "blk_1", "blk_2"))
    placed = (P(BLK, GRP), P(GRP, BLK), P(), P(), P())
    return jax.shard_map(
        shards, mesh=split, in_specs=placed, out_specs=P(None, GRP, None, BLK), check_vma=False
    )
```

```python
import functools

import jax
import jax.numpy as jnp
from jax import lax
from jax.experimental import pallas as pl
from jax.experimental.pallas import tpu as pltpu
from jax.sharding import Mesh
from jax.sharding import PartitionSpec as P

BS = 128
BLK = ("blk_0", "blk_1", "blk_2")
GRP = ("grp_0", "grp_1")
TILE = 256


def expand_kernel(row_blocks, slots_ref, left_ref, right_ref, out_ref):
    step = pl.program_id(0)
    product = jnp.dot(left_ref[...], right_ref[...], preferred_element_type=jnp.float32)
    per_tile = TILE // BS
    for r in range(row_blocks):
        for t in range(per_tile):
            slot = slots_ref[r, step * per_tile + t]

            @pl.when(slot >= 0)
            def _():
                out_ref[pl.ds(r * BS, BS), pl.ds(pl.multiple_of(slot * BS, BS), BS)] = product[
                    r * BS:(r + 1) * BS, t * BS:(t + 1) * BS
                ]


def expand_packed(slots, left, right, half_blocks):
    rows, inner = left.shape
    width = right.shape[1]
    row_blocks = rows // BS
    return pl.pallas_call(
        functools.partial(expand_kernel, row_blocks),
        out_shape=jax.ShapeDtypeStruct((rows, half_blocks * BS), jnp.float32),
        grid_spec=pltpu.PrefetchScalarGridSpec(
            num_scalar_prefetch=1,
            grid=(width // TILE,),
            in_specs=[
                pl.BlockSpec((rows, inner), lambda i, s: (0, 0), pipeline_mode=pl.Buffered(1)),
                pl.BlockSpec((inner, TILE), lambda i, s: (0, i)),
            ],
            out_specs=pl.BlockSpec(
                (rows, half_blocks * BS), lambda i, s: (0, 0), pipeline_mode=pl.Buffered(1)
            ),
        ),
        compiler_params=pltpu.CompilerParams(
            dimension_semantics=("arbitrary",), vmem_limit_bytes=48 * 1024 * 1024
        ),
        cost_estimate=pl.CostEstimate(
            flops=2 * rows * inner * width,
            transcendentals=0,
            bytes_accessed=rows * inner * 2 + inner * width * 2 + rows * half_blocks * BS * 4,
        ),
    )(slots, left, right)


def shards(matrix, panels, pattern, pruned, owners):
    blk_count = lax.axis_size(BLK)
    blk_id = lax.axis_index(BLK)
    grp_id = lax.axis_index(GRP)
    row_count, inner = matrix.shape
    panel_width = panels.shape[1]
    row_blocks = row_count // BS
    inner_blocks = inner // BS
    panel_blocks = panel_width // BS
    width_total = panel_width * blk_count
    window_blocks = width_total // BS
    half_blocks = window_blocks // 2
    tile_left = lax.dynamic_slice(
        pattern, (blk_id * row_blocks, grp_id * inner_blocks), (row_blocks, inner_blocks)
    ).astype(jnp.bfloat16)
    left = (matrix.reshape(row_blocks, BS, inner_blocks, BS) * tile_left[:, None, :, None]).reshape(
        row_count, inner
    )
    tile_right = lax.dynamic_slice(
        pattern, (grp_id * inner_blocks, blk_id * panel_blocks), (inner_blocks, panel_blocks)
    ).astype(jnp.bfloat16)
    right = (
        panels.reshape(inner_blocks, BS, panel_blocks, BS) * tile_right[:, None, :, None]
    ).reshape(inner, panel_width)
    gathered = lax.all_gather(right, BLK, axis=1, tiled=True)
    local_pruned = lax.dynamic_slice_in_dim(pruned, blk_id * row_blocks, row_blocks, 0)
    local_slots = jnp.clip(jnp.cumsum(local_pruned, axis=1) - 1, 0, half_blocks - 1)
    slot_table = jnp.where(local_pruned > 0, local_slots, -1).astype(jnp.int32)
    packed = expand_packed(slot_table, left, gathered, half_blocks)
    summed_packed = lax.psum_scatter(packed, GRP, scatter_dimension=0, tiled=True)
    piece_rows = row_count // lax.axis_size(GRP)
    row_block = (blk_id * row_count + grp_id * piece_rows) // BS
    row_pruned = lax.dynamic_index_in_dim(pruned, row_block, 0, keepdims=False)
    slot_of = jnp.clip(jnp.cumsum(row_pruned) - 1, 0, half_blocks - 1)
    squared = summed_packed.reshape(piece_rows, half_blocks, BS)
    squared = squared * squared
    inverse = (
        jnp.zeros((window_blocks,), jnp.int32)
        .at[owners]
        .set(jnp.arange(window_blocks, dtype=jnp.int32))
    )
    picked = jnp.take(squared, slot_of[inverse], axis=1)
    kept = picked * row_pruned[inverse].astype(jnp.float32)[None, :, None]
    arranged = kept.reshape(1, piece_rows, width_total)
    moved = lax.all_to_all(arranged, BLK, split_axis=2, concat_axis=0, tiled=True)
    totals = lax.psum(jnp.sum(moved, axis=(0, 1)), GRP)
    normalized = (row_count * blk_count) * moved / totals
    return normalized[:, None, :, :]


def solution(mesh):
    split = Mesh(mesh.devices.reshape(2, 4, 2, 4, 2), ("grp_0", "grp_1", "blk_0", "blk_1", "blk_2"))
    placed = (P(BLK, GRP), P(GRP, BLK), P(), P(), P())
    return jax.shard_map(
        shards, mesh=split, in_specs=placed, out_specs=P(None, GRP, None, BLK), check_vma=False
    )
```

```python
import functools

import jax
import jax.numpy as jnp
from jax import lax
from jax.experimental import pallas as pl
from jax.experimental.pallas import tpu as pltpu
from jax.sharding import Mesh
from jax.sharding import PartitionSpec as P

BS = 128
BLK = ("blk_0", "blk_1", "blk_2")
GRP = ("grp_0", "grp_1")
TILE = 256


def expand_kernel(row_blocks, slots_ref, left_ref, right_ref, out_ref):
    step = pl.program_id(0)
    product = jnp.dot(left_ref[...], right_ref[...], preferred_element_type=jnp.float32)
    per_tile = TILE // BS
    for r in range(row_blocks):
        for t in range(per_tile):
            slot = slots_ref[r, step * per_tile + t]

            @pl.when(slot >= 0)
            def _():
                out_ref[pl.ds(r * BS, BS), pl.ds(pl.multiple_of(slot * BS, BS), BS)] = product[
                    r * BS:(r + 1) * BS, t * BS:(t + 1) * BS
                ]


def expand_packed(slots, left, right, half_blocks):
    rows, inner = left.shape
    width = right.shape[1]
    row_blocks = rows // BS
    return pl.pallas_call(
        functools.partial(expand_kernel, row_blocks),
        out_shape=jax.ShapeDtypeStruct((rows, half_blocks * BS), jnp.float32),
        grid_spec=pltpu.PrefetchScalarGridSpec(
            num_scalar_prefetch=1,
            grid=(width // TILE,),
            in_specs=[
                pl.BlockSpec((rows, inner), lambda i, s: (0, 0), pipeline_mode=pl.Buffered(1)),
                pl.BlockSpec((inner, TILE), lambda i, s: (0, i)),
            ],
            out_specs=pl.BlockSpec(
                (rows, half_blocks * BS), lambda i, s: (0, 0), pipeline_mode=pl.Buffered(1)
            ),
        ),
        compiler_params=pltpu.CompilerParams(
            dimension_semantics=("arbitrary",), vmem_limit_bytes=48 * 1024 * 1024
        ),
        cost_estimate=pl.CostEstimate(
            flops=2 * rows * inner * width,
            transcendentals=0,
            bytes_accessed=rows * inner * 2 + inner * width * 2 + rows * half_blocks * BS * 4,
        ),
    )(slots, left, right)


def shards(matrix, panels, pattern, pruned, owners):
    blk_count = lax.axis_size(BLK)
    blk_id = lax.axis_index(BLK)
    grp_id = lax.axis_index(GRP)
    row_count, inner = matrix.shape
    panel_width = panels.shape[1]
    row_blocks = row_count // BS
    inner_blocks = inner // BS
    panel_blocks = panel_width // BS
    width_total = panel_width * blk_count
    window_blocks = width_total // BS
    half_blocks = window_blocks // 2
    tile_left = lax.dynamic_slice(
        pattern, (blk_id * row_blocks, grp_id * inner_blocks), (row_blocks, inner_blocks)
    ).astype(jnp.bfloat16)
    left = (matrix.reshape(row_blocks, BS, inner_blocks, BS) * tile_left[:, None, :, None]).reshape(
        row_count, inner
    )
    tile_right = lax.dynamic_slice(
        pattern, (grp_id * inner_blocks, blk_id * panel_blocks), (inner_blocks, panel_blocks)
    ).astype(jnp.bfloat16)
    right = (
        panels.reshape(inner_blocks, BS, panel_blocks, BS) * tile_right[:, None, :, None]
    ).reshape(inner, panel_width)
    gathered = lax.all_gather(right, BLK, axis=1, tiled=True)
    local_pruned = lax.dynamic_slice_in_dim(pruned, blk_id * row_blocks, row_blocks, 0)
    local_slots = jnp.clip(jnp.cumsum(local_pruned, axis=1) - 1, 0, half_blocks - 1)
    slot_table = jnp.where(local_pruned > 0, local_slots, -1).astype(jnp.int32)
    packed = expand_packed(slot_table, left, gathered, half_blocks)
    summed_packed = lax.psum_scatter(packed, GRP, scatter_dimension=0, tiled=True)
    piece_rows = row_count // lax.axis_size(GRP)
    row_block = (blk_id * row_count + grp_id * piece_rows) // BS
    row_pruned = lax.dynamic_index_in_dim(pruned, row_block, 0, keepdims=False)
    slot_of = jnp.clip(jnp.cumsum(row_pruned) - 1, 0, half_blocks - 1)
    squared = summed_packed.reshape(piece_rows, half_blocks, BS)
    squared = squared * squared
    inverse = (
        jnp.zeros((window_blocks,), jnp.int32)
        .at[owners]
        .set(jnp.arange(window_blocks, dtype=jnp.int32))
    )
    picked = jnp.take(squared, slot_of[inverse], axis=1)
    kept = picked * row_pruned[inverse].astype(jnp.float32)[None, :, None]
    arranged = kept.reshape(piece_rows, width_total)
    sums = jnp.zeros((8, width_total), jnp.float32).at[0].set(jnp.sum(arranged, axis=0))
    payload = jnp.concatenate([arranged, sums], axis=0)[None]
    moved = lax.all_to_all(payload, BLK, split_axis=2, concat_axis=0, tiled=True)
    totals = lax.psum(jnp.sum(moved[:, piece_rows, :], axis=0), GRP)
    normalized = (row_count * blk_count) * moved[:, :piece_rows, :] / totals
    return normalized[:, None, :, :]


def solution(mesh):
    split = Mesh(mesh.devices.reshape(2, 4, 2, 4, 2), ("grp_0", "grp_1", "blk_0", "blk_1", "blk_2"))
    placed = (P(BLK, GRP), P(GRP, BLK), P(), P(), P())
    return jax.shard_map(
        shards, mesh=split, in_specs=placed, out_specs=P(None, GRP, None, BLK), check_vma=False
    )
```

```python
import functools

import jax
import jax.numpy as jnp
from jax import lax
from jax.experimental import pallas as pl
from jax.experimental.pallas import tpu as pltpu
from jax.sharding import Mesh
from jax.sharding import PartitionSpec as P

BS = 128
BLK = ("blk_0", "blk_1", "blk_2")
GRP = ("grp_0", "grp_1")
TILE = 256


def expand_kernel(row_blocks, slots_ref, left_ref, right_ref, out_ref):
    step = pl.program_id(0)
    product = jnp.dot(left_ref[...], right_ref[...], preferred_element_type=jnp.float32)
    per_tile = TILE // BS
    for r in range(row_blocks):
        for t in range(per_tile):
            slot = slots_ref[r, step * per_tile + t]

            @pl.when(slot >= 0)
            def _():
                out_ref[pl.ds(r * BS, BS), pl.ds(pl.multiple_of(slot * BS, BS), BS)] = product[
                    r * BS:(r + 1) * BS, t * BS:(t + 1) * BS
                ]


def expand_packed(slots, left, right, half_blocks):
    rows, inner = left.shape
    width = right.shape[1]
    row_blocks = rows // BS
    return pl.pallas_call(
        functools.partial(expand_kernel, row_blocks),
        out_shape=jax.ShapeDtypeStruct((rows, half_blocks * BS), jnp.float32),
        grid_spec=pltpu.PrefetchScalarGridSpec(
            num_scalar_prefetch=1,
            grid=(width // TILE,),
            in_specs=[
                pl.BlockSpec((rows, inner), lambda i, s: (0, 0), pipeline_mode=pl.Buffered(1)),
                pl.BlockSpec((inner, TILE), lambda i, s: (0, i)),
            ],
            out_specs=pl.BlockSpec(
                (rows, half_blocks * BS), lambda i, s: (0, 0), pipeline_mode=pl.Buffered(1)
            ),
        ),
        compiler_params=pltpu.CompilerParams(
            dimension_semantics=("arbitrary",), vmem_limit_bytes=48 * 1024 * 1024
        ),
        cost_estimate=pl.CostEstimate(
            flops=2 * rows * inner * width,
            transcendentals=0,
            bytes_accessed=rows * inner * 2 + inner * width * 2 + rows * half_blocks * BS * 4,
        ),
    )(slots, left, right)


def shards(matrix, panels, pattern, pruned, owners):
    blk_count = lax.axis_size(BLK)
    blk_id = lax.axis_index(BLK)
    grp_id = lax.axis_index(GRP)
    row_count, inner = matrix.shape
    panel_width = panels.shape[1]
    row_blocks = row_count // BS
    inner_blocks = inner // BS
    panel_blocks = panel_width // BS
    width_total = panel_width * blk_count
    window_blocks = width_total // BS
    half_blocks = window_blocks // 2
    tile_left = lax.dynamic_slice(
        pattern, (blk_id * row_blocks, grp_id * inner_blocks), (row_blocks, inner_blocks)
    ).astype(jnp.bfloat16)
    left = (matrix.reshape(row_blocks, BS, inner_blocks, BS) * tile_left[:, None, :, None]).reshape(
        row_count, inner
    )
    tile_right = lax.dynamic_slice(
        pattern, (grp_id * inner_blocks, blk_id * panel_blocks), (inner_blocks, panel_blocks)
    ).astype(jnp.bfloat16)
    right = (
        panels.reshape(inner_blocks, BS, panel_blocks, BS) * tile_right[:, None, :, None]
    ).reshape(inner, panel_width)
    gathered = lax.all_gather(right, BLK, axis=1, tiled=True)
    local_pruned = lax.dynamic_slice_in_dim(pruned, blk_id * row_blocks, row_blocks, 0)
    local_slots = jnp.clip(jnp.cumsum(local_pruned, axis=1) - 1, 0, half_blocks - 1)
    slot_table = jnp.where(local_pruned > 0, local_slots, -1).astype(jnp.int32)
    packed = expand_packed(slot_table, left, gathered, half_blocks)
    summed_packed = lax.psum_scatter(packed, GRP, scatter_dimension=0, tiled=True)
    piece_rows = row_count // lax.axis_size(GRP)
    row_block = (blk_id * row_count + grp_id * piece_rows) // BS
    row_pruned = lax.dynamic_index_in_dim(pruned, row_block, 0, keepdims=False)
    slot_of = jnp.clip(jnp.cumsum(row_pruned) - 1, 0, half_blocks - 1)
    squared = summed_packed.reshape(piece_rows, half_blocks, BS)
    squared = squared * squared
    inverse = (
        jnp.zeros((window_blocks,), jnp.int32)
        .at[owners]
        .set(jnp.arange(window_blocks, dtype=jnp.int32))
    )
    picked = jnp.take(squared, slot_of[inverse], axis=1)
    kept = picked * row_pruned[inverse].astype(jnp.float32)[None, :, None]
    arranged = (
        kept.reshape(piece_rows, blk_count, window_blocks // blk_count, BS)
        .transpose(1, 0, 2, 3)
        .reshape(blk_count, piece_rows, panel_width)
    )
    moved = lax.all_to_all(arranged, BLK, split_axis=0, concat_axis=0, tiled=True)
    totals = lax.psum(jnp.sum(moved, axis=(0, 1)), GRP)
    normalized = (row_count * blk_count) * moved / totals
    return normalized[:, None, :, :]


def solution(mesh):
    split = Mesh(mesh.devices.reshape(2, 4, 2, 4, 2), ("grp_0", "grp_1", "blk_0", "blk_1", "blk_2"))
    placed = (P(BLK, GRP), P(GRP, BLK), P(), P(), P())
    return jax.shard_map(
        shards, mesh=split, in_specs=placed, out_specs=P(None, GRP, None, BLK), check_vma=False
    )
```

```python
import functools

import jax
import jax.numpy as jnp
from jax import lax
from jax.experimental import pallas as pl
from jax.experimental.pallas import tpu as pltpu
from jax.sharding import Mesh
from jax.sharding import PartitionSpec as P

BS = 128
BLK = ("blk_0", "blk_1", "blk_2")
GRP = ("grp_0", "grp_1")
TILE = 256


def expand_kernel(row_blocks, height, slots_ref, left_ref, right_ref, out_ref):
    step = pl.program_id(0)
    product = jnp.dot(left_ref[...], right_ref[...], preferred_element_type=jnp.float32)
    per_tile = TILE // BS
    for r in range(row_blocks):
        for t in range(per_tile):
            slot = slots_ref[r, step * per_tile + t]

            @pl.when(slot >= 0)
            def _():
                out_ref[pl.ds(r * height, height), pl.ds(pl.multiple_of(slot * BS, BS), BS)] = product[
                    r * height:(r + 1) * height, t * BS:(t + 1) * BS
                ]


def expand_packed(slots, left, right, half_blocks):
    rows, inner = left.shape
    width = right.shape[1]
    row_blocks = slots.shape[0]
    return pl.pallas_call(
        functools.partial(expand_kernel, row_blocks, rows // row_blocks),
        out_shape=jax.ShapeDtypeStruct((rows, half_blocks * BS), jnp.float32),
        grid_spec=pltpu.PrefetchScalarGridSpec(
            num_scalar_prefetch=1,
            grid=(width // TILE,),
            in_specs=[
                pl.BlockSpec((rows, inner), lambda i, s: (0, 0), pipeline_mode=pl.Buffered(1)),
                pl.BlockSpec((inner, TILE), lambda i, s: (0, i)),
            ],
            out_specs=pl.BlockSpec(
                (rows, half_blocks * BS), lambda i, s: (0, 0), pipeline_mode=pl.Buffered(1)
            ),
        ),
        compiler_params=pltpu.CompilerParams(
            dimension_semantics=("arbitrary",), vmem_limit_bytes=48 * 1024 * 1024
        ),
        cost_estimate=pl.CostEstimate(
            flops=2 * rows * inner * width,
            transcendentals=0,
            bytes_accessed=rows * inner * 2 + inner * width * 2 + rows * half_blocks * BS * 4,
        ),
    )(slots, left, right)


def shards(matrix, panels, pattern, pruned, owners):
    blk_count = lax.axis_size(BLK)
    blk_id = lax.axis_index(BLK)
    grp_id = lax.axis_index(GRP)
    row_count, inner = matrix.shape
    panel_width = panels.shape[1]
    row_blocks = row_count // BS
    inner_blocks = inner // BS
    panel_blocks = panel_width // BS
    width_total = panel_width * blk_count
    window_blocks = width_total // BS
    half_blocks = window_blocks // 2
    tile_left = lax.dynamic_slice(
        pattern, (blk_id * row_blocks, grp_id * inner_blocks), (row_blocks, inner_blocks)
    ).astype(jnp.bfloat16)
    left = (matrix.reshape(row_blocks, BS, inner_blocks, BS) * tile_left[:, None, :, None]).reshape(
        row_count, inner
    )
    tile_right = lax.dynamic_slice(
        pattern, (grp_id * inner_blocks, blk_id * panel_blocks), (inner_blocks, panel_blocks)
    ).astype(jnp.bfloat16)
    right = (
        panels.reshape(inner_blocks, BS, panel_blocks, BS) * tile_right[:, None, :, None]
    ).reshape(inner, panel_width)
    gathered = lax.all_gather(right, BLK, axis=1, tiled=True)
    local_pruned = lax.dynamic_slice_in_dim(pruned, blk_id * row_blocks, row_blocks, 0)
    local_slots = jnp.clip(jnp.cumsum(local_pruned, axis=1) - 1, 0, half_blocks - 1)
    slot_table = jnp.where(local_pruned > 0, local_slots, -1).astype(jnp.int32)
    piece_rows = row_count // lax.axis_size(GRP)
    row_block = (blk_id * row_count + grp_id * piece_rows) // BS
    row_pruned = lax.dynamic_index_in_dim(pruned, row_block, 0, keepdims=False)
    slot_of = jnp.clip(jnp.cumsum(row_pruned) - 1, 0, half_blocks - 1)
    inverse = (
        jnp.zeros((window_blocks,), jnp.int32)
        .at[owners]
        .set(jnp.arange(window_blocks, dtype=jnp.int32))
    )
    halves = 2
    half_rows = piece_rows // halves
    split_left = left.reshape(row_blocks, halves, BS // halves, inner)
    def expand(h):
        part_left = split_left[:, h].reshape(row_count // halves, inner)
        return expand_packed(slot_table, part_left, gathered, half_blocks)

    def arrange(summed_packed):
        squared = summed_packed.reshape(half_rows, half_blocks, BS)
        squared = squared * squared
        picked = jnp.take(squared, slot_of[inverse], axis=1)
        kept = picked * row_pruned[inverse].astype(jnp.float32)[None, :, None]
        return (
            kept.reshape(half_rows, blk_count, window_blocks // blk_count, BS)
            .transpose(1, 0, 2, 3)
            .reshape(blk_count, half_rows, panel_width)
        )

    moved_parts = []
    packed = expand(0)
    for h in range(halves):
        summed_packed = lax.psum_scatter(packed, GRP, scatter_dimension=0, tiled=True)
        if h + 1 < halves:
            packed = expand(h + 1)
        arranged = arrange(summed_packed)
        if h + 1 < halves:
            arranged, packed = lax.optimization_barrier((arranged, packed))
        moved_parts.append(lax.all_to_all(arranged, BLK, split_axis=0, concat_axis=0, tiled=True))
    moved = jnp.concatenate(moved_parts, axis=1)
    local_sums = sum(jnp.sum(part, axis=(0, 1)) for part in moved_parts)
    totals = lax.psum(local_sums, GRP)
    normalized = (row_count * blk_count) * moved / totals
    return normalized[:, None, :, :]


def solution(mesh):
    split = Mesh(mesh.devices.reshape(2, 4, 2, 4, 2), ("grp_0", "grp_1", "blk_0", "blk_1", "blk_2"))
    placed = (P(BLK, GRP), P(GRP, BLK), P(), P(), P())
    return jax.shard_map(
        shards, mesh=split, in_specs=placed, out_specs=P(None, GRP, None, BLK), check_vma=False
    )
```

```python
import functools

import jax
import jax.numpy as jnp
from jax import lax
from jax.experimental import pallas as pl
from jax.experimental.pallas import tpu as pltpu
from jax.sharding import Mesh
from jax.sharding import PartitionSpec as P

BS = 128
BLK = ("blk_0", "blk_1", "blk_2")
GRP = ("grp_0", "grp_1")
TILE = 256


def expand_kernel(row_blocks, slots_ref, left_ref, right_ref, out_ref):
    step = pl.program_id(0)
    product = jnp.dot(left_ref[...], right_ref[...], preferred_element_type=jnp.float32)
    per_tile = TILE // BS
    for r in range(row_blocks):
        for t in range(per_tile):
            slot = slots_ref[r, step * per_tile + t]

            @pl.when(slot >= 0)
            def _():
                out_ref[pl.ds(r * BS, BS), pl.ds(pl.multiple_of(slot * BS, BS), BS)] = product[
                    r * BS:(r + 1) * BS, t * BS:(t + 1) * BS
                ]


def expand_packed(slots, left, right, half_blocks):
    rows, inner = left.shape
    width = right.shape[1]
    row_blocks = rows // BS
    return pl.pallas_call(
        functools.partial(expand_kernel, row_blocks),
        out_shape=jax.ShapeDtypeStruct((rows, half_blocks * BS), jnp.float32),
        grid_spec=pltpu.PrefetchScalarGridSpec(
            num_scalar_prefetch=1,
            grid=(width // TILE,),
            in_specs=[
                pl.BlockSpec((rows, inner), lambda i, s: (0, 0), pipeline_mode=pl.Buffered(1)),
                pl.BlockSpec((inner, TILE), lambda i, s: (0, i)),
            ],
            out_specs=pl.BlockSpec(
                (rows, half_blocks * BS), lambda i, s: (0, 0), pipeline_mode=pl.Buffered(1)
            ),
        ),
        compiler_params=pltpu.CompilerParams(
            dimension_semantics=("arbitrary",), vmem_limit_bytes=48 * 1024 * 1024
        ),
        cost_estimate=pl.CostEstimate(
            flops=2 * rows * inner * width,
            transcendentals=0,
            bytes_accessed=rows * inner * 2 + inner * width * 2 + rows * half_blocks * BS * 4,
        ),
    )(slots, left, right)


def shards(matrix, panels, pattern, pruned, owners):
    blk_count = lax.axis_size(BLK)
    blk_id = lax.axis_index(BLK)
    grp_id = lax.axis_index(GRP)
    row_count, inner = matrix.shape
    panel_width = panels.shape[1]
    row_blocks = row_count // BS
    inner_blocks = inner // BS
    panel_blocks = panel_width // BS
    width_total = panel_width * blk_count
    window_blocks = width_total // BS
    half_blocks = window_blocks // 2
    tile_left = lax.dynamic_slice(
        pattern, (blk_id * row_blocks, grp_id * inner_blocks), (row_blocks, inner_blocks)
    ).astype(jnp.bfloat16)
    left = (matrix.reshape(row_blocks, BS, inner_blocks, BS) * tile_left[:, None, :, None]).reshape(
        row_count, inner
    )
    tile_right = lax.dynamic_slice(
        pattern, (grp_id * inner_blocks, blk_id * panel_blocks), (inner_blocks, panel_blocks)
    ).astype(jnp.bfloat16)
    right = (
        panels.reshape(inner_blocks, BS, panel_blocks, BS) * tile_right[:, None, :, None]
    ).reshape(inner, panel_width)
    gathered = lax.all_gather(right, BLK, axis=1, tiled=True)
    local_pruned = lax.dynamic_slice_in_dim(pruned, blk_id * row_blocks, row_blocks, 0)
    local_slots = jnp.clip(jnp.cumsum(local_pruned, axis=1) - 1, 0, half_blocks - 1)
    slot_table = jnp.where(local_pruned > 0, local_slots, -1).astype(jnp.int32)
    packed = expand_packed(slot_table, left, gathered, half_blocks)
    summed_packed = lax.psum_scatter(packed, GRP, scatter_dimension=0, tiled=True)
    piece_rows = row_count // lax.axis_size(GRP)
    row_block = (blk_id * row_count + grp_id * piece_rows) // BS
    row_pruned = lax.dynamic_index_in_dim(pruned, row_block, 0, keepdims=False)
    slot_of = jnp.clip(jnp.cumsum(row_pruned) - 1, 0, half_blocks - 1)
    squared = summed_packed.reshape(piece_rows, half_blocks, BS)
    squared = squared * squared
    inverse = (
        jnp.zeros((window_blocks,), jnp.int32)
        .at[owners]
        .set(jnp.arange(window_blocks, dtype=jnp.int32))
    )
    picked = jnp.take(squared, slot_of[inverse], axis=1)
    kept = picked * row_pruned[inverse].astype(jnp.float32)[None, :, None]
    arranged = (
        kept.reshape(piece_rows, blk_count, window_blocks // blk_count, BS)
        .transpose(1, 0, 2, 3)
        .reshape(blk_count, piece_rows, panel_width)
    )
    moved = lax.all_to_all(arranged, BLK, split_axis=0, concat_axis=0, tiled=True)
    group_sums = lax.psum(jnp.sum(arranged, axis=1), GRP)
    group_sums, moved = lax.optimization_barrier((group_sums, moved))
    owner_sums = lax.all_to_all(group_sums, BLK, split_axis=0, concat_axis=0, tiled=True)
    totals = jnp.sum(owner_sums, axis=0)
    normalized = (row_count * blk_count) * moved / totals
    return normalized[:, None, :, :]


def solution(mesh):
    split = Mesh(mesh.devices.reshape(2, 4, 2, 4, 2), ("grp_0", "grp_1", "blk_0", "blk_1", "blk_2"))
    placed = (P(BLK, GRP), P(GRP, BLK), P(), P(), P())
    return jax.shard_map(
        shards, mesh=split, in_specs=placed, out_specs=P(None, GRP, None, BLK), check_vma=False
    )
```

```python
import functools

import jax
import jax.numpy as jnp
from jax import lax
from jax.experimental import pallas as pl
from jax.experimental.pallas import tpu as pltpu
from jax.sharding import Mesh
from jax.sharding import PartitionSpec as P

BS = 128
BLK = ("blk_0", "blk_1", "blk_2")
GRP = ("grp_0", "grp_1")
TILE = 256


def expand_kernel(row_blocks, order, slots_ref, left_ref, right_ref, out_ref):
    step = pl.program_id(0)
    product = jnp.dot(left_ref[...], right_ref[...], preferred_element_type=jnp.float32)
    per_tile = TILE // BS
    for r in range(row_blocks):
        for t in range(per_tile):
            slot = slots_ref[r, step * per_tile + t]

            @pl.when(slot >= 0)
            def _():
                out_ref[pl.ds(order[r] * BS, BS), pl.ds(pl.multiple_of(slot * BS, BS), BS)] = product[
                    r * BS:(r + 1) * BS, t * BS:(t + 1) * BS
                ]


def expand_packed(slots, left, right, half_blocks, order):
    rows, inner = left.shape
    width = right.shape[1]
    row_blocks = rows // BS
    return pl.pallas_call(
        functools.partial(expand_kernel, row_blocks, order),
        out_shape=jax.ShapeDtypeStruct((rows, half_blocks * BS), jnp.float32),
        grid_spec=pltpu.PrefetchScalarGridSpec(
            num_scalar_prefetch=1,
            grid=(width // TILE,),
            in_specs=[
                pl.BlockSpec((rows, inner), lambda i, s: (0, 0), pipeline_mode=pl.Buffered(1)),
                pl.BlockSpec((inner, TILE), lambda i, s: (0, i)),
            ],
            out_specs=pl.BlockSpec(
                (rows, half_blocks * BS), lambda i, s: (0, 0), pipeline_mode=pl.Buffered(1)
            ),
        ),
        compiler_params=pltpu.CompilerParams(
            dimension_semantics=("arbitrary",), vmem_limit_bytes=48 * 1024 * 1024
        ),
        cost_estimate=pl.CostEstimate(
            flops=2 * rows * inner * width,
            transcendentals=0,
            bytes_accessed=rows * inner * 2 + inner * width * 2 + rows * half_blocks * BS * 4,
        ),
    )(slots, left, right)


def shards(matrix, panels, pattern, pruned, owners):
    blk_count = lax.axis_size(BLK)
    blk_id = lax.axis_index(BLK)
    grp_id = lax.axis_index(GRP)
    row_count, inner = matrix.shape
    panel_width = panels.shape[1]
    row_blocks = row_count // BS
    inner_blocks = inner // BS
    panel_blocks = panel_width // BS
    width_total = panel_width * blk_count
    window_blocks = width_total // BS
    half_blocks = window_blocks // 2
    tile_left = lax.dynamic_slice(
        pattern, (blk_id * row_blocks, grp_id * inner_blocks), (row_blocks, inner_blocks)
    ).astype(jnp.bfloat16)
    left = (matrix.reshape(row_blocks, BS, inner_blocks, BS) * tile_left[:, None, :, None]).reshape(
        row_count, inner
    )
    tile_right = lax.dynamic_slice(
        pattern, (grp_id * inner_blocks, blk_id * panel_blocks), (inner_blocks, panel_blocks)
    ).astype(jnp.bfloat16)
    right = (
        panels.reshape(inner_blocks, BS, panel_blocks, BS) * tile_right[:, None, :, None]
    ).reshape(inner, panel_width)
    gathered = lax.all_gather(right, BLK, axis=1, tiled=True)
    local_pruned = lax.dynamic_slice_in_dim(pruned, blk_id * row_blocks, row_blocks, 0)
    local_slots = jnp.clip(jnp.cumsum(local_pruned, axis=1) - 1, 0, half_blocks - 1)
    slot_table = jnp.where(local_pruned > 0, local_slots, -1).astype(jnp.int32)
    z_size = lax.axis_size(GRP[0])
    x_size = lax.axis_size(GRP[1])
    order = tuple((r % x_size) * z_size + r // x_size for r in range(row_blocks))
    packed = expand_packed(slot_table, left, gathered, half_blocks, order)
    staged = lax.psum_scatter(packed, GRP[1], scatter_dimension=0, tiled=True)
    summed_packed = lax.psum_scatter(staged, GRP[0], scatter_dimension=0, tiled=True)
    piece_rows = row_count // lax.axis_size(GRP)
    row_block = (blk_id * row_count + grp_id * piece_rows) // BS
    row_pruned = lax.dynamic_index_in_dim(pruned, row_block, 0, keepdims=False)
    slot_of = jnp.clip(jnp.cumsum(row_pruned) - 1, 0, half_blocks - 1)
    squared = summed_packed.reshape(piece_rows, half_blocks, BS)
    squared = squared * squared
    inverse = (
        jnp.zeros((window_blocks,), jnp.int32)
        .at[owners]
        .set(jnp.arange(window_blocks, dtype=jnp.int32))
    )
    picked = jnp.take(squared, slot_of[inverse], axis=1)
    kept = picked * row_pruned[inverse].astype(jnp.float32)[None, :, None]
    arranged = (
        kept.reshape(piece_rows, blk_count, window_blocks // blk_count, BS)
        .transpose(1, 0, 2, 3)
        .reshape(blk_count, piece_rows, panel_width)
    )
    moved = lax.all_to_all(arranged, BLK, split_axis=0, concat_axis=0, tiled=True)
    totals = lax.psum(jnp.sum(moved, axis=(0, 1)), GRP)
    normalized = (row_count * blk_count) * moved / totals
    return normalized[:, None, :, :]


def solution(mesh):
    split = Mesh(mesh.devices.reshape(2, 4, 2, 4, 2), ("grp_0", "grp_1", "blk_0", "blk_1", "blk_2"))
    placed = (P(BLK, GRP), P(GRP, BLK), P(), P(), P())
    return jax.shard_map(
        shards, mesh=split, in_specs=placed, out_specs=P(None, GRP, None, BLK), check_vma=False
    )
```

```python
import functools

import jax
import jax.numpy as jnp
from jax import lax
from jax.experimental import pallas as pl
from jax.experimental.pallas import tpu as pltpu
from jax.sharding import Mesh
from jax.sharding import PartitionSpec as P

BS = 128
BLK = ("blk_0", "blk_1", "blk_2")
GRP = ("grp_0", "grp_1")
TILE = 512


def expand_kernel(row_blocks, slots_ref, left_ref, right_ref, out_ref):
    step = pl.program_id(0)
    product = jnp.dot(left_ref[...], right_ref[...], preferred_element_type=jnp.float32)
    per_tile = TILE // BS
    for r in range(row_blocks):
        for t in range(per_tile):
            slot = slots_ref[r, step * per_tile + t]

            @pl.when(slot >= 0)
            def _():
                out_ref[pl.ds(r * BS, BS), pl.ds(pl.multiple_of(slot * BS, BS), BS)] = product[
                    r * BS:(r + 1) * BS, t * BS:(t + 1) * BS
                ]


def expand_packed(slots, left, right, half_blocks):
    rows, inner = left.shape
    width = right.shape[1]
    row_blocks = rows // BS
    return pl.pallas_call(
        functools.partial(expand_kernel, row_blocks),
        out_shape=jax.ShapeDtypeStruct((rows, half_blocks * BS), jnp.float32),
        grid_spec=pltpu.PrefetchScalarGridSpec(
            num_scalar_prefetch=1,
            grid=(width // TILE,),
            in_specs=[
                pl.BlockSpec((rows, inner), lambda i, s: (0, 0), pipeline_mode=pl.Buffered(1)),
                pl.BlockSpec((inner, TILE), lambda i, s: (0, i)),
            ],
            out_specs=pl.BlockSpec(
                (rows, half_blocks * BS), lambda i, s: (0, 0), pipeline_mode=pl.Buffered(1)
            ),
        ),
        compiler_params=pltpu.CompilerParams(
            dimension_semantics=("arbitrary",), vmem_limit_bytes=48 * 1024 * 1024
        ),
        cost_estimate=pl.CostEstimate(
            flops=2 * rows * inner * width,
            transcendentals=0,
            bytes_accessed=rows * inner * 2 + inner * width * 2 + rows * half_blocks * BS * 4,
        ),
    )(slots, left, right)


def shards(matrix, panels, pattern, pruned, owners):
    blk_count = lax.axis_size(BLK)
    blk_id = lax.axis_index(BLK)
    grp_id = lax.axis_index(GRP)
    row_count, inner = matrix.shape
    panel_width = panels.shape[1]
    row_blocks = row_count // BS
    inner_blocks = inner // BS
    panel_blocks = panel_width // BS
    width_total = panel_width * blk_count
    window_blocks = width_total // BS
    half_blocks = window_blocks // 2
    tile_left = lax.dynamic_slice(
        pattern, (blk_id * row_blocks, grp_id * inner_blocks), (row_blocks, inner_blocks)
    ).astype(jnp.bfloat16)
    left = (matrix.reshape(row_blocks, BS, inner_blocks, BS) * tile_left[:, None, :, None]).reshape(
        row_count, inner
    )
    tile_right = lax.dynamic_slice(
        pattern, (grp_id * inner_blocks, blk_id * panel_blocks), (inner_blocks, panel_blocks)
    ).astype(jnp.bfloat16)
    right = (
        panels.reshape(inner_blocks, BS, panel_blocks, BS) * tile_right[:, None, :, None]
    ).reshape(inner, panel_width)
    gathered = lax.all_gather(right, BLK, axis=1, tiled=True)
    local_pruned = lax.dynamic_slice_in_dim(pruned, blk_id * row_blocks, row_blocks, 0)
    local_slots = jnp.clip(jnp.cumsum(local_pruned, axis=1) - 1, 0, half_blocks - 1)
    slot_table = jnp.where(local_pruned > 0, local_slots, -1).astype(jnp.int32)
    packed = expand_packed(slot_table, left, gathered, half_blocks)
    summed_packed = lax.psum_scatter(packed, GRP, scatter_dimension=0, tiled=True)
    piece_rows = row_count // lax.axis_size(GRP)
    row_block = (blk_id * row_count + grp_id * piece_rows) // BS
    row_pruned = lax.dynamic_index_in_dim(pruned, row_block, 0, keepdims=False)
    slot_of = jnp.clip(jnp.cumsum(row_pruned) - 1, 0, half_blocks - 1)
    squared = summed_packed.reshape(piece_rows, half_blocks, BS)
    squared = squared * squared
    inverse = (
        jnp.zeros((window_blocks,), jnp.int32)
        .at[owners]
        .set(jnp.arange(window_blocks, dtype=jnp.int32))
    )
    picked = jnp.take(squared, slot_of[inverse], axis=1)
    kept = picked * row_pruned[inverse].astype(jnp.float32)[None, :, None]
    arranged = (
        kept.reshape(piece_rows, blk_count, window_blocks // blk_count, BS)
        .transpose(1, 0, 2, 3)
        .reshape(blk_count, piece_rows, panel_width)
    )
    moved = lax.all_to_all(arranged, BLK, split_axis=0, concat_axis=0, tiled=True)
    totals = lax.psum(jnp.sum(moved, axis=(0, 1)), GRP)
    normalized = (row_count * blk_count) * moved / totals
    return normalized[:, None, :, :]


def solution(mesh):
    split = Mesh(mesh.devices.reshape(2, 4, 2, 4, 2), ("grp_0", "grp_1", "blk_0", "blk_1", "blk_2"))
    placed = (P(BLK, GRP), P(GRP, BLK), P(), P(), P())
    return jax.shard_map(
        shards, mesh=split, in_specs=placed, out_specs=P(None, GRP, None, BLK), check_vma=False
    )
```

```python
import functools

import jax
import jax.numpy as jnp
from jax import lax
from jax.experimental import pallas as pl
from jax.experimental.pallas import tpu as pltpu
from jax.sharding import Mesh
from jax.sharding import PartitionSpec as P

BS = 128
BLK = ("blk_0", "blk_1", "blk_2")
GRP = ("grp_0", "grp_1")
TILE = 512


def expand_kernel(row_blocks, slots_ref, left_ref, right_ref, out_ref):
    step = pl.program_id(0)
    product = jnp.dot(left_ref[...], right_ref[...], preferred_element_type=jnp.float32)
    per_tile = TILE // BS
    for r in range(row_blocks):
        for t in range(per_tile):
            slot = slots_ref[r, step * per_tile + t]

            @pl.when(slot >= 0)
            def _():
                out_ref[pl.ds(r * BS, BS), pl.ds(pl.multiple_of(slot * BS, BS), BS)] = product[
                    r * BS:(r + 1) * BS, t * BS:(t + 1) * BS
                ]


def expand_packed(slots, left, right, half_blocks):
    rows, inner = left.shape
    width = right.shape[1]
    row_blocks = rows // BS
    return pl.pallas_call(
        functools.partial(expand_kernel, row_blocks),
        out_shape=jax.ShapeDtypeStruct((rows, half_blocks * BS), jnp.float32),
        grid_spec=pltpu.PrefetchScalarGridSpec(
            num_scalar_prefetch=1,
            grid=(width // TILE,),
            in_specs=[
                pl.BlockSpec((rows, inner), lambda i, s: (0, 0), pipeline_mode=pl.Buffered(1)),
                pl.BlockSpec((inner, TILE), lambda i, s: (0, i)),
            ],
            out_specs=pl.BlockSpec(
                (rows, half_blocks * BS), lambda i, s: (0, 0), pipeline_mode=pl.Buffered(1)
            ),
        ),
        compiler_params=pltpu.CompilerParams(
            dimension_semantics=("arbitrary",), vmem_limit_bytes=48 * 1024 * 1024
        ),
        cost_estimate=pl.CostEstimate(
            flops=2 * rows * inner * width,
            transcendentals=0,
            bytes_accessed=rows * inner * 2 + inner * width * 2 + rows * half_blocks * BS * 4,
        ),
    )(slots, left, right)


def shards(matrix, panels, pattern, pruned, owners):
    blk_count = lax.axis_size(BLK)
    blk_id = lax.axis_index(BLK)
    grp_id = lax.axis_index(GRP)
    row_count, inner = matrix.shape
    panel_width = panels.shape[1]
    row_blocks = row_count // BS
    inner_blocks = inner // BS
    panel_blocks = panel_width // BS
    width_total = panel_width * blk_count
    window_blocks = width_total // BS
    half_blocks = window_blocks // 2
    tile_left = lax.dynamic_slice(
        pattern, (blk_id * row_blocks, grp_id * inner_blocks), (row_blocks, inner_blocks)
    ).astype(jnp.bfloat16)
    left = (matrix.reshape(row_blocks, BS, inner_blocks, BS) * tile_left[:, None, :, None]).reshape(
        row_count, inner
    )
    tile_right = lax.dynamic_slice(
        pattern, (grp_id * inner_blocks, blk_id * panel_blocks), (inner_blocks, panel_blocks)
    ).astype(jnp.bfloat16)
    right = (
        panels.reshape(inner_blocks, BS, panel_blocks, BS) * tile_right[:, None, :, None]
    ).reshape(inner, panel_width)
    gathered = lax.all_gather(right, BLK, axis=1, tiled=True)
    local_pruned = lax.dynamic_slice_in_dim(pruned, blk_id * row_blocks, row_blocks, 0)
    local_slots = jnp.clip(jnp.cumsum(local_pruned, axis=1) - 1, 0, half_blocks - 1)
    slot_table = jnp.where(local_pruned > 0, local_slots, -1).astype(jnp.int32)
    packed = expand_packed(slot_table, left, gathered, half_blocks)
    summed_packed = lax.psum_scatter(packed, GRP, scatter_dimension=0, tiled=True)
    piece_rows = row_count // lax.axis_size(GRP)
    row_block = (blk_id * row_count + grp_id * piece_rows) // BS
    row_pruned = lax.dynamic_index_in_dim(pruned, row_block, 0, keepdims=False)
    slot_of = jnp.clip(jnp.cumsum(row_pruned) - 1, 0, half_blocks - 1)
    squared = summed_packed.reshape(piece_rows, half_blocks, BS)
    squared = squared * squared
    inverse = (
        jnp.zeros((window_blocks,), jnp.int32)
        .at[owners]
        .set(jnp.arange(window_blocks, dtype=jnp.int32))
    )
    picked = jnp.take(squared, slot_of[inverse], axis=1)
    kept = picked * row_pruned[inverse].astype(jnp.float32)[None, :, None]
    arranged = (
        kept.reshape(piece_rows, blk_count, window_blocks // blk_count, BS)
        .transpose(1, 0, 2, 3)
        .reshape(blk_count, piece_rows, panel_width)
    )
    moved = lax.all_to_all(arranged, BLK, split_axis=0, concat_axis=0, tiled=True)
    totals = jnp.sum(lax.all_gather(jnp.sum(moved, axis=(0, 1)), GRP), axis=0)
    normalized = (row_count * blk_count) * moved / totals
    return normalized[:, None, :, :]


def solution(mesh):
    split = Mesh(mesh.devices.reshape(2, 4, 2, 4, 2), ("grp_0", "grp_1", "blk_0", "blk_1", "blk_2"))
    placed = (P(BLK, GRP), P(GRP, BLK), P(), P(), P())
    return jax.shard_map(
        shards, mesh=split, in_specs=placed, out_specs=P(None, GRP, None, BLK), check_vma=False
    )
```

```python
import functools

import jax
import jax.numpy as jnp
from jax import lax
from jax.experimental import pallas as pl
from jax.experimental.pallas import tpu as pltpu
from jax.sharding import Mesh
from jax.sharding import PartitionSpec as P

BS = 128
BLK = ("blk_0", "blk_1", "blk_2")
GRP = ("grp_0", "grp_1")
TILE = 256


def expand_kernel(row_blocks, slots_ref, pieces_ref, left_ref, first_ref, second_ref, out_ref):
    del pieces_ref
    step = pl.program_id(0)
    split = first_ref.shape[0]
    product = jnp.dot(left_ref[:, :split], first_ref[...], preferred_element_type=jnp.float32)
    product += jnp.dot(left_ref[:, split:], second_ref[...], preferred_element_type=jnp.float32)
    per_tile = TILE // BS
    for r in range(row_blocks):
        for t in range(per_tile):
            slot = slots_ref[r, step * per_tile + t]

            @pl.when(slot >= 0)
            def _():
                out_ref[pl.ds(r * BS, BS), pl.ds(pl.multiple_of(slot * BS, BS), BS)] = product[
                    r * BS:(r + 1) * BS, t * BS:(t + 1) * BS
                ]


def expand_packed(slots, pieces, left, first, second, half_blocks):
    rows, inner = left.shape
    split, width = first.shape
    row_blocks = rows // BS
    return pl.pallas_call(
        functools.partial(expand_kernel, row_blocks),
        out_shape=jax.ShapeDtypeStruct((rows, half_blocks * BS), jnp.float32),
        grid_spec=pltpu.PrefetchScalarGridSpec(
            num_scalar_prefetch=2,
            grid=(width // TILE,),
            in_specs=[
                pl.BlockSpec((rows, inner), lambda i, s, p: (0, 0), pipeline_mode=pl.Buffered(1)),
                pl.BlockSpec((split, TILE), lambda i, s, p: (0, i)),
                pl.BlockSpec((None, inner - split, TILE), lambda i, s, p: (p[i], 0, 0)),
            ],
            out_specs=pl.BlockSpec(
                (rows, half_blocks * BS), lambda i, s, p: (0, 0), pipeline_mode=pl.Buffered(1)
            ),
        ),
        compiler_params=pltpu.CompilerParams(
            dimension_semantics=("arbitrary",), vmem_limit_bytes=48 * 1024 * 1024
        ),
        cost_estimate=pl.CostEstimate(
            flops=2 * rows * inner * width,
            transcendentals=0,
            bytes_accessed=rows * inner * 2 + inner * width * 2 + rows * half_blocks * BS * 4,
        ),
    )(slots, pieces, left, first, second)


def shards(matrix, panels, pattern, pruned, owners):
    blk_count = lax.axis_size(BLK)
    blk_id = lax.axis_index(BLK)
    grp_id = lax.axis_index(GRP)
    row_count, inner = matrix.shape
    panel_width = panels.shape[1]
    row_blocks = row_count // BS
    inner_blocks = inner // BS
    panel_blocks = panel_width // BS
    width_total = panel_width * blk_count
    window_blocks = width_total // BS
    half_blocks = window_blocks // 2
    tile_left = lax.dynamic_slice(
        pattern, (blk_id * row_blocks, grp_id * inner_blocks), (row_blocks, inner_blocks)
    ).astype(jnp.bfloat16)
    left = (matrix.reshape(row_blocks, BS, inner_blocks, BS) * tile_left[:, None, :, None]).reshape(
        row_count, inner
    )
    tile_right = lax.dynamic_slice(
        pattern, (grp_id * inner_blocks, blk_id * panel_blocks), (inner_blocks, panel_blocks)
    ).astype(jnp.bfloat16)
    right = (
        panels.reshape(inner_blocks, BS, panel_blocks, BS) * tile_right[:, None, :, None]
    ).reshape(inner, panel_width)
    split = inner // 2
    first = lax.all_gather(right[:split], BLK, axis=1, tiled=True)
    second_part = right[split:]
    pieces = [second_part] + [
        lax.ppermute(second_part, BLK, [(i, (i + k) % blk_count) for i in range(blk_count)])
        for k in range(1, blk_count)
    ]
    second = jnp.stack(pieces)
    piece_of = ((blk_id - jnp.arange(blk_count, dtype=jnp.int32)) % blk_count).astype(jnp.int32)
    local_pruned = lax.dynamic_slice_in_dim(pruned, blk_id * row_blocks, row_blocks, 0)
    local_slots = jnp.clip(jnp.cumsum(local_pruned, axis=1) - 1, 0, half_blocks - 1)
    slot_table = jnp.where(local_pruned > 0, local_slots, -1).astype(jnp.int32)
    packed = expand_packed(slot_table, piece_of, left, first, second, half_blocks)
    summed_packed = lax.psum_scatter(packed, GRP, scatter_dimension=0, tiled=True)
    piece_rows = row_count // lax.axis_size(GRP)
    row_block = (blk_id * row_count + grp_id * piece_rows) // BS
    row_pruned = lax.dynamic_index_in_dim(pruned, row_block, 0, keepdims=False)
    slot_of = jnp.clip(jnp.cumsum(row_pruned) - 1, 0, half_blocks - 1)
    squared = summed_packed.reshape(piece_rows, half_blocks, BS)
    squared = squared * squared
    inverse = (
        jnp.zeros((window_blocks,), jnp.int32)
        .at[owners]
        .set(jnp.arange(window_blocks, dtype=jnp.int32))
    )
    picked = jnp.take(squared, slot_of[inverse], axis=1)
    kept = picked * row_pruned[inverse].astype(jnp.float32)[None, :, None]
    arranged = (
        kept.reshape(piece_rows, blk_count, window_blocks // blk_count, BS)
        .transpose(1, 0, 2, 3)
        .reshape(blk_count, piece_rows, panel_width)
    )
    moved = lax.all_to_all(arranged, BLK, split_axis=0, concat_axis=0, tiled=True)
    totals = jnp.sum(lax.all_gather(jnp.sum(moved, axis=(0, 1)), GRP), axis=0)
    normalized = (row_count * blk_count) * moved / totals
    return normalized[:, None, :, :]


def solution(mesh):
    split = Mesh(mesh.devices.reshape(2, 4, 2, 4, 2), ("grp_0", "grp_1", "blk_0", "blk_1", "blk_2"))
    placed = (P(BLK, GRP), P(GRP, BLK), P(), P(), P())
    return jax.shard_map(
        shards, mesh=split, in_specs=placed, out_specs=P(None, GRP, None, BLK), check_vma=False
    )
```

```python
import functools

import jax
import jax.numpy as jnp
from jax import lax
from jax.experimental import pallas as pl
from jax.experimental.pallas import tpu as pltpu
from jax.sharding import Mesh
from jax.sharding import PartitionSpec as P

BS = 128
BLK = ("blk_0", "blk_1", "blk_2")
GRP = ("grp_0", "grp_1")
TILE = 512


def expand_kernel(row_blocks, slots_ref, left_ref, right_ref, out_ref):
    step = pl.program_id(0)
    product = jnp.dot(left_ref[...], right_ref[...], preferred_element_type=jnp.float32)
    per_tile = TILE // BS
    for r in range(row_blocks):
        for t in range(per_tile):
            slot = slots_ref[r, step * per_tile + t]

            @pl.when(slot >= 0)
            def _():
                out_ref[pl.ds(r * BS, BS), pl.ds(pl.multiple_of(slot * BS, BS), BS)] = product[
                    r * BS:(r + 1) * BS, t * BS:(t + 1) * BS
                ]


def expand_packed(slots, left, right, half_blocks):
    rows, inner = left.shape
    width = right.shape[1]
    row_blocks = rows // BS
    return pl.pallas_call(
        functools.partial(expand_kernel, row_blocks),
        out_shape=jax.ShapeDtypeStruct((rows, half_blocks * BS), jnp.float32),
        grid_spec=pltpu.PrefetchScalarGridSpec(
            num_scalar_prefetch=1,
            grid=(width // TILE,),
            in_specs=[
                pl.BlockSpec((rows, inner), lambda i, s: (0, 0), pipeline_mode=pl.Buffered(1)),
                pl.BlockSpec((inner, TILE), lambda i, s: (0, i)),
            ],
            out_specs=pl.BlockSpec(
                (rows, half_blocks * BS), lambda i, s: (0, 0), pipeline_mode=pl.Buffered(1)
            ),
        ),
        compiler_params=pltpu.CompilerParams(
            dimension_semantics=("arbitrary",), vmem_limit_bytes=48 * 1024 * 1024
        ),
        cost_estimate=pl.CostEstimate(
            flops=2 * rows * inner * width,
            transcendentals=0,
            bytes_accessed=rows * inner * 2 + inner * width * 2 + rows * half_blocks * BS * 4,
        ),
    )(slots, left, right)


def shards(matrix, panels, pattern, pruned, owners):
    blk_count = lax.axis_size(BLK)
    blk_id = lax.axis_index(BLK)
    grp_id = lax.axis_index(GRP)
    row_count, inner = matrix.shape
    panel_width = panels.shape[1]
    row_blocks = row_count // BS
    inner_blocks = inner // BS
    panel_blocks = panel_width // BS
    width_total = panel_width * blk_count
    window_blocks = width_total // BS
    half_blocks = window_blocks // 2
    tile_left = lax.dynamic_slice(
        pattern, (blk_id * row_blocks, grp_id * inner_blocks), (row_blocks, inner_blocks)
    ).astype(jnp.bfloat16)
    left = (matrix.reshape(row_blocks, BS, inner_blocks, BS) * tile_left[:, None, :, None]).reshape(
        row_count, inner
    )
    tile_right = lax.dynamic_slice(
        pattern, (grp_id * inner_blocks, blk_id * panel_blocks), (inner_blocks, panel_blocks)
    ).astype(jnp.bfloat16)
    right = (
        panels.reshape(inner_blocks, BS, panel_blocks, BS) * tile_right[:, None, :, None]
    ).reshape(inner, panel_width)
    gathered = lax.all_gather(right, BLK, axis=1, tiled=True)
    local_pruned = lax.dynamic_slice_in_dim(pruned, blk_id * row_blocks, row_blocks, 0)
    local_slots = jnp.clip(jnp.cumsum(local_pruned, axis=1) - 1, 0, half_blocks - 1)
    slot_table = jnp.where(local_pruned > 0, local_slots, -1).astype(jnp.int32)
    packed = expand_packed(slot_table, left, gathered, half_blocks)
    summed_packed = lax.psum_scatter(packed, GRP, scatter_dimension=0, tiled=True)
    piece_rows = row_count // lax.axis_size(GRP)
    row_block = (blk_id * row_count + grp_id * piece_rows) // BS
    row_pruned = lax.dynamic_index_in_dim(pruned, row_block, 0, keepdims=False)
    slot_of = jnp.clip(jnp.cumsum(row_pruned) - 1, 0, half_blocks - 1)
    squared = summed_packed.reshape(piece_rows, half_blocks, BS)
    squared = squared * squared
    inverse = (
        jnp.zeros((window_blocks,), jnp.int32)
        .at[owners]
        .set(jnp.arange(window_blocks, dtype=jnp.int32))
    )
    picked = jnp.take(squared, slot_of[inverse], axis=1)
    kept = picked * row_pruned[inverse].astype(jnp.float32)[None, :, None]
    arranged = (
        kept.reshape(piece_rows, blk_count, window_blocks // blk_count, BS)
        .transpose(1, 0, 2, 3)
        .reshape(blk_count, piece_rows, panel_width)
    )
    moved = lax.all_to_all(arranged, BLK, split_axis=0, concat_axis=0, tiled=True)
    group_sums = lax.psum(jnp.sum(arranged, axis=1), GRP)
    totals = lax.psum_scatter(group_sums, BLK, scatter_dimension=0, tiled=True)
    normalized = (row_count * blk_count) * moved / totals
    return normalized[:, None, :, :]


def solution(mesh):
    split = Mesh(mesh.devices.reshape(2, 4, 2, 4, 2), ("grp_0", "grp_1", "blk_0", "blk_1", "blk_2"))
    placed = (P(BLK, GRP), P(GRP, BLK), P(), P(), P())
    return jax.shard_map(
        shards, mesh=split, in_specs=placed, out_specs=P(None, GRP, None, BLK), check_vma=False
    )
```

```python
import functools

import jax
import jax.numpy as jnp
from jax import lax
from jax.experimental import pallas as pl
from jax.experimental.pallas import tpu as pltpu
from jax.sharding import Mesh
from jax.sharding import PartitionSpec as P

BS = 128
BLK = ("blk_0", "blk_1", "blk_2")
GRP = ("grp_0", "grp_1")
TILE = 512


def expand_kernel(row_blocks, slots_ref, left_ref, right_ref, out_ref):
    step = pl.program_id(0)
    product = jnp.dot(left_ref[...], right_ref[...], preferred_element_type=jnp.float32)
    per_tile = TILE // BS
    for r in range(row_blocks):
        for t in range(per_tile):
            slot = slots_ref[r, step * per_tile + t]

            @pl.when(slot >= 0)
            def _():
                out_ref[pl.ds(r * BS, BS), pl.ds(pl.multiple_of(slot * BS, BS), BS)] = product[
                    r * BS:(r + 1) * BS, t * BS:(t + 1) * BS
                ]


def expand_packed(slots, left, right, half_blocks):
    rows, inner = left.shape
    width = right.shape[1]
    row_blocks = rows // BS
    return pl.pallas_call(
        functools.partial(expand_kernel, row_blocks),
        out_shape=jax.ShapeDtypeStruct((rows, half_blocks * BS), jnp.float32),
        grid_spec=pltpu.PrefetchScalarGridSpec(
            num_scalar_prefetch=1,
            grid=(width // TILE,),
            in_specs=[
                pl.BlockSpec((rows, inner), lambda i, s: (0, 0), pipeline_mode=pl.Buffered(1)),
                pl.BlockSpec((inner, TILE), lambda i, s: (0, i)),
            ],
            out_specs=pl.BlockSpec(
                (rows, half_blocks * BS), lambda i, s: (0, 0), pipeline_mode=pl.Buffered(1)
            ),
        ),
        compiler_params=pltpu.CompilerParams(
            dimension_semantics=("arbitrary",), vmem_limit_bytes=48 * 1024 * 1024
        ),
        cost_estimate=pl.CostEstimate(
            flops=2 * rows * inner * width,
            transcendentals=0,
            bytes_accessed=rows * inner * 2 + inner * width * 2 + rows * half_blocks * BS * 4,
        ),
    )(slots, left, right)


def shards(matrix, panels, pattern, pruned, owners):
    blk_count = lax.axis_size(BLK)
    blk_id = lax.axis_index(BLK)
    grp_id = lax.axis_index(GRP)
    row_count, inner = matrix.shape
    panel_width = panels.shape[1]
    row_blocks = row_count // BS
    inner_blocks = inner // BS
    panel_blocks = panel_width // BS
    width_total = panel_width * blk_count
    window_blocks = width_total // BS
    half_blocks = window_blocks // 2
    tile_left = lax.dynamic_slice(
        pattern, (blk_id * row_blocks, grp_id * inner_blocks), (row_blocks, inner_blocks)
    ).astype(jnp.bfloat16)
    left = (matrix.reshape(row_blocks, BS, inner_blocks, BS) * tile_left[:, None, :, None]).reshape(
        row_count, inner
    )
    tile_right = lax.dynamic_slice(
        pattern, (grp_id * inner_blocks, blk_id * panel_blocks), (inner_blocks, panel_blocks)
    )
    keep_right = jnp.repeat(jnp.repeat(tile_right > 0, BS, axis=0), BS, axis=1)
    right = jnp.where(keep_right, panels, jnp.zeros_like(panels))
    gathered = lax.all_gather(right, BLK, axis=1, tiled=True)
    local_pruned = lax.dynamic_slice_in_dim(pruned, blk_id * row_blocks, row_blocks, 0)
    local_slots = jnp.clip(jnp.cumsum(local_pruned, axis=1) - 1, 0, half_blocks - 1)
    slot_table = jnp.where(local_pruned > 0, local_slots, -1).astype(jnp.int32)
    packed = expand_packed(slot_table, left, gathered, half_blocks)
    summed_packed = lax.psum_scatter(packed, GRP, scatter_dimension=0, tiled=True)
    piece_rows = row_count // lax.axis_size(GRP)
    row_block = (blk_id * row_count + grp_id * piece_rows) // BS
    row_pruned = lax.dynamic_index_in_dim(pruned, row_block, 0, keepdims=False)
    slot_of = jnp.clip(jnp.cumsum(row_pruned) - 1, 0, half_blocks - 1)
    squared = summed_packed.reshape(piece_rows, half_blocks, BS)
    squared = squared * squared
    inverse = (
        jnp.zeros((window_blocks,), jnp.int32)
        .at[owners]
        .set(jnp.arange(window_blocks, dtype=jnp.int32))
    )
    picked = jnp.take(squared, slot_of[inverse], axis=1)
    kept = picked * row_pruned[inverse].astype(jnp.float32)[None, :, None]
    arranged = (
        kept.reshape(piece_rows, blk_count, window_blocks // blk_count, BS)
        .transpose(1, 0, 2, 3)
        .reshape(blk_count, piece_rows, panel_width)
    )
    moved = lax.all_to_all(arranged, BLK, split_axis=0, concat_axis=0, tiled=True)
    totals = jnp.sum(lax.all_gather(jnp.sum(moved, axis=(0, 1)), GRP), axis=0)
    normalized = (row_count * blk_count) * moved / totals
    return normalized[:, None, :, :]


def solution(mesh):
    split = Mesh(mesh.devices.reshape(2, 4, 2, 4, 2), ("grp_0", "grp_1", "blk_0", "blk_1", "blk_2"))
    placed = (P(BLK, GRP), P(GRP, BLK), P(), P(), P())
    return jax.shard_map(
        shards, mesh=split, in_specs=placed, out_specs=P(None, GRP, None, BLK), check_vma=False
    )
```

```python
import functools

import jax
import jax.numpy as jnp
from jax import lax
from jax.experimental import pallas as pl
from jax.experimental.pallas import tpu as pltpu
from jax.sharding import Mesh
from jax.sharding import PartitionSpec as P

BS = 128
BLK = ("blk_0", "blk_1", "blk_2")
GRP = ("grp_0", "grp_1")
TILE = 512


def expand_kernel(row_blocks, slots_ref, left_ref, right_ref, out_ref):
    step = pl.program_id(0)
    product = jnp.dot(left_ref[...], right_ref[...], preferred_element_type=jnp.float32)
    per_tile = TILE // BS
    for r in range(row_blocks):
        for t in range(per_tile):
            slot = slots_ref[r, step * per_tile + t]

            @pl.when(slot >= 0)
            def _():
                out_ref[pl.ds(r * BS, BS), pl.ds(pl.multiple_of(slot * BS, BS), BS)] = product[
                    r * BS:(r + 1) * BS, t * BS:(t + 1) * BS
                ]


def expand_packed(slots, left, right, half_blocks):
    rows, inner = left.shape
    width = right.shape[1]
    row_blocks = rows // BS
    return pl.pallas_call(
        functools.partial(expand_kernel, row_blocks),
        out_shape=jax.ShapeDtypeStruct((rows, half_blocks * BS), jnp.float32),
        grid_spec=pltpu.PrefetchScalarGridSpec(
            num_scalar_prefetch=1,
            grid=(width // TILE,),
            in_specs=[
                pl.BlockSpec((rows, inner), lambda i, s: (0, 0), pipeline_mode=pl.Buffered(1)),
                pl.BlockSpec((inner, TILE), lambda i, s: (0, i)),
            ],
            out_specs=pl.BlockSpec(
                (rows, half_blocks * BS), lambda i, s: (0, 0), pipeline_mode=pl.Buffered(1)
            ),
        ),
        compiler_params=pltpu.CompilerParams(
            dimension_semantics=("arbitrary",), vmem_limit_bytes=48 * 1024 * 1024
        ),
        cost_estimate=pl.CostEstimate(
            flops=2 * rows * inner * width,
            transcendentals=0,
            bytes_accessed=rows * inner * 2 + inner * width * 2 + rows * half_blocks * BS * 4,
        ),
    )(slots, left, right)


def shards(matrix, panels, pattern, pruned, owners):
    blk_count = lax.axis_size(BLK)
    blk_id = lax.axis_index(BLK)
    grp_id = lax.axis_index(GRP)
    row_count, inner = matrix.shape
    panel_width = panels.shape[1]
    row_blocks = row_count // BS
    inner_blocks = inner // BS
    panel_blocks = panel_width // BS
    width_total = panel_width * blk_count
    window_blocks = width_total // BS
    half_blocks = window_blocks // 2
    tile_left = lax.dynamic_slice(
        pattern, (blk_id * row_blocks, grp_id * inner_blocks), (row_blocks, inner_blocks)
    ).astype(jnp.bfloat16)
    left = (matrix.reshape(row_blocks, BS, inner_blocks, BS) * tile_left[:, None, :, None]).reshape(
        row_count, inner
    )
    tile_right = lax.dynamic_slice(
        pattern, (grp_id * inner_blocks, blk_id * panel_blocks), (inner_blocks, panel_blocks)
    ).astype(jnp.bfloat16)
    right = (
        panels.reshape(inner_blocks, BS, panel_blocks, BS) * tile_right[:, None, :, None]
    ).reshape(inner, panel_width)
    gathered = lax.all_gather(right, BLK, axis=1, tiled=True)
    local_pruned = lax.dynamic_slice_in_dim(pruned, blk_id * row_blocks, row_blocks, 0)
    local_slots = jnp.clip(jnp.cumsum(local_pruned, axis=1) - 1, 0, half_blocks - 1)
    slot_table = jnp.where(local_pruned > 0, local_slots, -1).astype(jnp.int32)
    packed = expand_packed(slot_table, left, gathered, half_blocks)
    summed_packed = lax.psum_scatter(packed, GRP, scatter_dimension=0, tiled=True)
    piece_rows = row_count // lax.axis_size(GRP)
    row_block = (blk_id * row_count + grp_id * piece_rows) // BS
    row_pruned = lax.dynamic_index_in_dim(pruned, row_block, 0, keepdims=False)
    slot_of = jnp.clip(jnp.cumsum(row_pruned) - 1, 0, half_blocks - 1)
    squared = summed_packed.reshape(piece_rows, half_blocks, BS)
    squared = squared * squared
    inverse = (
        jnp.zeros((window_blocks,), jnp.int32)
        .at[owners]
        .set(jnp.arange(window_blocks, dtype=jnp.int32))
    )
    picked = jnp.take(squared, slot_of[inverse], axis=1)
    kept = picked * row_pruned[inverse].astype(jnp.float32)[None, :, None]
    arranged = (
        kept.reshape(piece_rows, blk_count, window_blocks // blk_count, BS)
        .transpose(1, 0, 2, 3)
        .reshape(blk_count, piece_rows, panel_width)
    )
    cores = lax.axis_size(BLK[2])
    chips = blk_count // cores
    moved = lax.all_to_all(
        arranged.reshape(chips, cores, piece_rows, panel_width), BLK[:2], 0, 0, tiled=True
    )
    moved = lax.all_to_all(moved.transpose(1, 0, 2, 3), BLK[2], 0, 0, tiled=True)
    moved = moved.transpose(1, 0, 2, 3).reshape(blk_count, piece_rows, panel_width)
    totals = jnp.sum(lax.all_gather(jnp.sum(moved, axis=(0, 1)), GRP), axis=0)
    normalized = (row_count * blk_count) * moved / totals
    return normalized[:, None, :, :]


def solution(mesh):
    split = Mesh(mesh.devices.reshape(2, 4, 2, 4, 2), ("grp_0", "grp_1", "blk_0", "blk_1", "blk_2"))
    placed = (P(BLK, GRP), P(GRP, BLK), P(), P(), P())
    return jax.shard_map(
        shards, mesh=split, in_specs=placed, out_specs=P(None, GRP, None, BLK), check_vma=False
    )
```

```python
import functools

import jax
import jax.numpy as jnp
from jax import lax
from jax.experimental import pallas as pl
from jax.experimental.pallas import tpu as pltpu
from jax.sharding import Mesh
from jax.sharding import PartitionSpec as P

BS = 128
BLK = ("blk_0", "blk_1", "blk_2")
GRP = ("grp_0", "grp_1")
TILE = 1024


def expand_kernel(row_blocks, slots_ref, left_ref, right_ref, out_ref):
    step = pl.program_id(0)
    product = jnp.dot(left_ref[...], right_ref[...], preferred_element_type=jnp.float32)
    per_tile = TILE // BS
    for r in range(row_blocks):
        for t in range(per_tile):
            slot = slots_ref[r, step * per_tile + t]

            @pl.when(slot >= 0)
            def _():
                out_ref[pl.ds(r * BS, BS), pl.ds(pl.multiple_of(slot * BS, BS), BS)] = product[
                    r * BS:(r + 1) * BS, t * BS:(t + 1) * BS
                ]


def expand_packed(slots, left, right, half_blocks):
    rows, inner = left.shape
    width = right.shape[1]
    row_blocks = rows // BS
    return pl.pallas_call(
        functools.partial(expand_kernel, row_blocks),
        out_shape=jax.ShapeDtypeStruct((rows, half_blocks * BS), jnp.float32),
        grid_spec=pltpu.PrefetchScalarGridSpec(
            num_scalar_prefetch=1,
            grid=(width // TILE,),
            in_specs=[
                pl.BlockSpec((rows, inner), lambda i, s: (0, 0), pipeline_mode=pl.Buffered(1)),
                pl.BlockSpec((inner, TILE), lambda i, s: (0, i)),
            ],
            out_specs=pl.BlockSpec(
                (rows, half_blocks * BS), lambda i, s: (0, 0), pipeline_mode=pl.Buffered(1)
            ),
        ),
        compiler_params=pltpu.CompilerParams(
            dimension_semantics=("arbitrary",), vmem_limit_bytes=48 * 1024 * 1024
        ),
        cost_estimate=pl.CostEstimate(
            flops=2 * rows * inner * width,
            transcendentals=0,
            bytes_accessed=rows * inner * 2 + inner * width * 2 + rows * half_blocks * BS * 4,
        ),
    )(slots, left, right)


def shards(matrix, panels, pattern, pruned, owners):
    blk_count = lax.axis_size(BLK)
    blk_id = lax.axis_index(BLK)
    grp_id = lax.axis_index(GRP)
    row_count, inner = matrix.shape
    panel_width = panels.shape[1]
    row_blocks = row_count // BS
    inner_blocks = inner // BS
    panel_blocks = panel_width // BS
    width_total = panel_width * blk_count
    window_blocks = width_total // BS
    half_blocks = window_blocks // 2
    tile_left = lax.dynamic_slice(
        pattern, (blk_id * row_blocks, grp_id * inner_blocks), (row_blocks, inner_blocks)
    ).astype(jnp.bfloat16)
    left = (matrix.reshape(row_blocks, BS, inner_blocks, BS) * tile_left[:, None, :, None]).reshape(
        row_count, inner
    )
    tile_right = lax.dynamic_slice(
        pattern, (grp_id * inner_blocks, blk_id * panel_blocks), (inner_blocks, panel_blocks)
    ).astype(jnp.bfloat16)
    right = (
        panels.reshape(inner_blocks, BS, panel_blocks, BS) * tile_right[:, None, :, None]
    ).reshape(inner, panel_width)
    gathered = lax.all_gather(right, BLK, axis=1, tiled=True)
    local_pruned = lax.dynamic_slice_in_dim(pruned, blk_id * row_blocks, row_blocks, 0)
    local_slots = jnp.clip(jnp.cumsum(local_pruned, axis=1) - 1, 0, half_blocks - 1)
    slot_table = jnp.where(local_pruned > 0, local_slots, -1).astype(jnp.int32)
    packed = expand_packed(slot_table, left, gathered, half_blocks)
    summed_packed = lax.psum_scatter(packed, GRP, scatter_dimension=0, tiled=True)
    piece_rows = row_count // lax.axis_size(GRP)
    row_block = (blk_id * row_count + grp_id * piece_rows) // BS
    row_pruned = lax.dynamic_index_in_dim(pruned, row_block, 0, keepdims=False)
    slot_of = jnp.clip(jnp.cumsum(row_pruned) - 1, 0, half_blocks - 1)
    squared = summed_packed.reshape(piece_rows, half_blocks, BS)
    squared = squared * squared
    inverse = (
        jnp.zeros((window_blocks,), jnp.int32)
        .at[owners]
        .set(jnp.arange(window_blocks, dtype=jnp.int32))
    )
    picked = jnp.take(squared, slot_of[inverse], axis=1)
    kept = picked * row_pruned[inverse].astype(jnp.float32)[None, :, None]
    arranged = (
        kept.reshape(piece_rows, blk_count, window_blocks // blk_count, BS)
        .transpose(1, 0, 2, 3)
        .reshape(blk_count, piece_rows, panel_width)
    )
    moved = lax.all_to_all(arranged, BLK, split_axis=0, concat_axis=0, tiled=True)
    totals = jnp.sum(lax.all_gather(jnp.sum(moved, axis=(0, 1)), GRP), axis=0)
    normalized = (row_count * blk_count) * moved / totals
    return normalized[:, None, :, :]


def solution(mesh):
    split = Mesh(mesh.devices.reshape(2, 4, 2, 4, 2), ("grp_0", "grp_1", "blk_0", "blk_1", "blk_2"))
    placed = (P(BLK, GRP), P(GRP, BLK), P(), P(), P())
    return jax.shard_map(
        shards, mesh=split, in_specs=placed, out_specs=P(None, GRP, None, BLK), check_vma=False
    )
```
